256 devices in a mesh: tf: 4 (over x), gz: 8 (over z), sec: 8 (over y, core).
Axes of the slice: x: 4, y: 4, z: 8, core: 2. Of those that a mesh axis runs over, the one named last changes fastest.
Arguments:
- residuals: bfloat16 [3, 4, 8, 8, 4, 8192], P(None, 'tf', 'gz', 'sec'), may hold values from -6 to 6
- weights: bfloat16 [4, 8, 8, 4, 8192], P('tf', 'gz', 'sec'), may hold values from 0.5 to 2
- fraction: bfloat16 [4, 8, 8, 4, 8192], P('tf', 'gz', 'sec'), may hold values from 0 to 1
- voxels: int32 [3, 4, 8, 8, 4, 8192], P(None, 'tf', 'gz', 'sec'), may hold values from 0 to 255, as said below
- kernel_reach: int32 [152], P('sec'), may hold values from 1 to 4
Outputs:
- distortion: float32 [3, 256, 152, 180], P(None, ('tf', 'gz'), 'sec')
The draws below stay inside these ranges and needn't reach their ends.
Inputs may be any that keep to these rules, and one draw needn't show every extreme that they name: `voxels`: component 0 is the pad row, 1 the pad bin, 2 the drift bin. A residual at sec index s has its row in s * 19 to s * 19 + 18; its pad bin is at most 178; a residual at gz index g in slot t of the fifth dimension has its drift bin in block t * (number of gz devices) + g, that is among the 8 bins from (t * (number of gz devices) + g) * 8 on.
All inputs are finite; a program needn't handle non-finite values.
Results may differ from the reference program's by a relative error of at most 0.0026.
Values may be sent and summed in bfloat16 or wider, within the bound.
No kernel may reach another device: no remote copies, remote signals or barrier semaphores. Data moves between devices by JAX's collectives and lax.ppermute only.
A program may use at most 64 MiB of HBM per device.

```python
import math
import jax
import jax.numpy as jnp
from jax import lax

ROWS = 152
PAD = 180
DRIFT = 256
RES_BLK = 8192
ROW_DEV = 19
DRIFT_DEV = 8
N_TF = 4
N_GZ = 8
N_SEC = 8


def draw_voxels(key, part):
    shape = (N_TF, N_GZ, N_SEC, N_TF, RES_BLK)
    first_key, second_key, third_key = jax.random.split(key, 3)
    gz_place = lax.broadcasted_iota(jnp.int32, shape, 1)
    sec_place = lax.broadcasted_iota(jnp.int32, shape, 2)
    target = lax.broadcasted_iota(jnp.int32, shape, 3)
    rows_at = sec_place * ROW_DEV + jax.random.randint(first_key, shape, 0, ROW_DEV)
    pads_at = jax.random.randint(second_key, shape, 0, PAD - 1)
    drift_at = (target * N_GZ + gz_place) * DRIFT_DEV + jax.random.randint(third_key, shape, 0, DRIFT_DEV)
    return jnp.stack([rows_at, pads_at, drift_at], 0).astype(jnp.int32)


def set_ends(array, own_key, low, top_value):
    spot = [jax.random.randint(jax.random.fold_in(own_key, axis), (), 0, length) for axis, length in enumerate(array.shape)]
    main_axis = array.shape.index(max(array.shape))
    neighbour = spot[:main_axis] + [(spot[main_axis] + 1) % array.shape[main_axis]] + spot[main_axis + 1:]
    return array.at[tuple(spot)].set(low).at[tuple(neighbour)].set(top_value)


def levels(key, dims, cuts, smallest, top_value):
    factor_of = 1.0
    for dim, blocks in cuts:
        steps = jax.random.uniform(jax.random.fold_in(jax.random.fold_in(key, 6), dim), (blocks,), jnp.float32, smallest / len(cuts), top_value / len(cuts))
        factor_of = factor_of * jnp.repeat(jnp.exp(steps), dims[dim] // blocks).reshape((-1,) + (1,) * (len(dims) - 1 - dim))
    return factor_of


def centred(rng, shape, deviation, bound, cuts=(), dtype=jnp.bfloat16):
    entries = jax.random.normal(rng, shape, jnp.float32) * deviation
    if len(cuts) > 0:
        entries = levels(rng, shape, cuts, -0.22, 0.18) * entries
    return jnp.clip(entries, min=-bound, max=bound).astype(dtype)


def setup_inputs(seed: int = 0) -> dict:
    key_of = jax.random.split(jax.random.key(seed), 6)
    return {
        "residuals": centred(key_of[0], (3, N_TF, N_GZ, N_SEC, N_TF, RES_BLK), 1.0, 6.0, ((1, 4), (2, 8), (3, 8))),
        "weights": jnp.clip(jnp.exp(math.log(2.0) - 1.3862944 * jax.random.uniform(key_of[1], (N_TF, N_GZ, N_SEC, N_TF, RES_BLK), jnp.float32) ** levels(key_of[1], (N_TF, N_GZ, N_SEC, N_TF, RES_BLK), ((0, 4), (1, 8), (2, 8)), -0.2, 0.2)), 0.5, 2.0).astype(jnp.bfloat16),
        "fraction": jnp.clip(1.0 * jax.random.uniform(key_of[2], (N_TF, N_GZ, N_SEC, N_TF, RES_BLK), jnp.float32) ** levels(key_of[2], (N_TF, N_GZ, N_SEC, N_TF, RES_BLK), ((0, 4), (1, 8), (2, 8)), -0.2, 0.2), 0.0, 1.0).astype(jnp.bfloat16),
        "voxels": draw_voxels(jax.random.fold_in(key_of[5], 71), 0),
        "kernel_reach": set_ends(jax.random.randint(key_of[4], (ROWS,), 1, 5), jax.random.fold_in(key_of[4], 1), 1, 4).astype(jnp.int32),
    }


def row_kernels(kernel_reach):
    spread = kernel_reach.astype(jnp.float32)[:, None, None]
    places = lax.broadcasted_iota(jnp.int32, (PAD, PAD), 0)
    others = lax.broadcasted_iota(jnp.int32, (PAD, PAD), 1)
    distance = jnp.abs(places - others).astype(jnp.float32)[None]
    return jnp.maximum(spread + 1.0 - distance, 0.0) / ((spread + 1.0) * (spread + 1.0))


def reference(residuals, weights, fraction, voxels, kernel_reach):
    components = residuals.reshape(3, -1).astype(jnp.float32)
    weight_all = weights.reshape(-1).astype(jnp.float32)
    share_all = fraction.reshape(-1).astype(jnp.float32)
    coords = voxels.reshape(3, -1)
    left_share = weight_all * (1.0 - share_all)
    right_share = weight_all * share_all
    left_chan = jnp.stack([left_share, left_share * components[0], left_share * components[1], left_share * components[2]], 1).astype(jnp.bfloat16)
    right_chan = jnp.stack([right_share, right_share * components[0], right_share * components[1], right_share * components[2]], 1).astype(jnp.bfloat16)
    left_chan, right_chan = lax.optimization_barrier((left_chan, right_chan))
    deposit = jnp.concatenate([left_chan.astype(jnp.float32), right_chan.astype(jnp.float32)], 0)
    flat = ((coords[2] * ROWS + coords[0]) * PAD + coords[1]).astype(jnp.int32)
    segment = jnp.concatenate([flat, flat + 1]).astype(jnp.int32)
    histogram = jax.ops.segment_sum(deposit, segment, num_segments=DRIFT * ROWS * PAD)
    histogram = histogram.reshape(DRIFT, ROWS, PAD, 4)
    means = histogram[..., 1:4] / (histogram[..., 0:1] + 1.0)
    means = jnp.transpose(means, (3, 0, 1, 2))
    across = jnp.einsum("kzrq,rpq->kzrp", means, row_kernels(kernel_reach), precision=lax.Precision.HIGHEST)
    padded = jnp.pad(across, ((0, 0), (0, 0), (2, 2), (0, 0)))
    smoothed = (padded[:, :, 0:ROWS] + 2.0 * padded[:, :, 1:ROWS + 1] + 3.0 * padded[:, :, 2:ROWS + 2]
                + 2.0 * padded[:, :, 3:ROWS + 3] + padded[:, :, 4:ROWS + 4]) / 9.0
    return jnp.cumsum(smoothed, axis=1)
```

```python
import functools

import jax
import jax.numpy as jnp
from jax import lax
from jax.experimental import pallas as pl
from jax.experimental.pallas import tpu as pltpu
from jax.sharding import PartitionSpec as P

PAD = 180
DRIFT = 256
PAD_SLOT = 192
CHUNK = 512


def with_halo(block, sides, width):
    for axis, dim in sides:
        count = lax.axis_size(axis)
        forward = [(i, i + 1) for i in range(count - 1)]
        backward = [(target, source) for source, target in forward]
        low = lax.ppermute(
            lax.slice_in_dim(block, block.shape[dim] - width, None, axis=dim), axis, forward
        )
        high = lax.ppermute(lax.slice_in_dim(block, 0, width, axis=dim), axis, backward)
        block = jnp.concatenate([low, block, high], axis=dim)
    return block


def row_kernels(kernel_reach):
    spread = kernel_reach.astype(jnp.float32)[:, None, None]
    places = lax.broadcasted_iota(jnp.int32, (PAD, PAD), 0)
    others = lax.broadcasted_iota(jnp.int32, (PAD, PAD), 1)
    distance = jnp.abs(places - others).astype(jnp.float32)[None]
    return jnp.maximum(spread + 1.0 - distance, 0.0) / ((spread + 1.0) * (spread + 1.0))


def hist_kernel(cell_rows, idx_ref, dep_ref, out_ref):
    source = pl.program_id(0)

    @pl.when(source == 0)
    def _():
        out_ref[...] = jnp.zeros_like(out_ref)

    length = idx_ref.shape[2]

    def body(step, carry):
        off = pl.multiple_of(step * CHUNK, CHUNK)
        cell = idx_ref[0, 0:1, pl.ds(off, CHUNK)]
        pad = idx_ref[0, 1:2, pl.ds(off, CHUNK)]
        dep = dep_ref[0, :, pl.ds(off, CHUNK)]
        c_iota = lax.broadcasted_iota(jnp.int32, (cell_rows, CHUNK), 0)
        onehot = jnp.where(c_iota == cell, 1.0, 0.0).astype(jnp.bfloat16)
        p_iota = lax.broadcasted_iota(jnp.int32, (PAD_SLOT, CHUNK), 0)
        at_left = p_iota == pad
        at_right = p_iota == pad + 1
        parts = []
        for k in range(4):
            parts.append(
                jnp.where(at_left, dep[k : k + 1], jnp.where(at_right, dep[4 + k : 5 + k], 0.0))
            )
        spread = jnp.concatenate(parts, 0).astype(jnp.bfloat16)
        out_ref[...] += lax.dot_general(
            onehot, spread, (((1,), (1,)), ((), ())), preferred_element_type=jnp.float32
        )
        return carry

    lax.fori_loop(0, length // CHUNK, body, 0)


def build_histogram(idx, dep, cell_rows):
    sources, _, length = idx.shape
    flops = 2 * cell_rows * 4 * PAD_SLOT * sources * length
    return pl.pallas_call(
        functools.partial(hist_kernel, cell_rows),
        out_shape=jax.ShapeDtypeStruct((cell_rows, 4 * PAD_SLOT), jnp.float32),
        grid=(sources,),
        in_specs=[
            pl.BlockSpec((1, 2, length), lambda s: (s, 0, 0)),
            pl.BlockSpec((1, 8, length), lambda s: (s, 0, 0)),
        ],
        out_specs=pl.BlockSpec((cell_rows, 4 * PAD_SLOT), lambda s: (0, 0)),
        compiler_params=pltpu.CompilerParams(dimension_semantics=("arbitrary",)),
        cost_estimate=pl.CostEstimate(
            flops=flops,
            transcendentals=0,
            bytes_accessed=sources * length * 40 + cell_rows * 4 * PAD_SLOT * 4,
        ),
    )(idx, dep)


def exclusive_prefix(totals):
    gz_count = lax.axis_size("gz")
    tf_count = lax.axis_size("tf")
    g = lax.axis_index("gz")
    before = jnp.zeros_like(totals)
    row_sum = totals
    for shift in range(1, gz_count):
        pairs = [(i, (i + shift) % gz_count) for i in range(gz_count)]
        got = lax.ppermute(totals, "gz", pairs)
        row_sum = row_sum + got
        before = before + jnp.where(shift <= g, got, 0.0)
    for shift in range(1, tf_count):
        pairs = [(i, i + shift) for i in range(tf_count - shift)]
        before = before + lax.ppermute(row_sum, "tf", pairs)
    return before


def smooth(field, kernel_reach):
    across = jnp.einsum(
        "kzrq,rpq->kzrp", field, row_kernels(kernel_reach), precision=lax.Precision.HIGHEST
    )
    rimmed = with_halo(across, (("sec", 2),), 2)
    row_total = across.shape[2]
    return (
        rimmed[:, :, 0:row_total]
        + 2.0 * rimmed[:, :, 1 : row_total + 1]
        + 3.0 * rimmed[:, :, 2 : row_total + 2]
        + 2.0 * rimmed[:, :, 3 : row_total + 3]
        + rimmed[:, :, 4 : row_total + 4]
    ) / 9.0


def per_device(residuals, weights, fraction, voxels, kernel_reach):
    gz_count = lax.axis_size("gz")
    drift_dev = DRIFT // (lax.axis_size("tf") * gz_count)
    row_dev = kernel_reach.shape[0]
    cell_count = drift_dev * row_dev
    cell_rows = -(-cell_count // 16) * 16
    coords = voxels[:, 0, 0, 0]
    target = lax.broadcasted_iota(jnp.int32, coords.shape[1:], 0)
    local_row = coords[0] - lax.axis_index("sec") * row_dev
    local_drift = coords[2] - (target * gz_count + lax.axis_index("gz")) * drift_dev
    cell = local_drift * row_dev + local_row
    outgoing = jnp.concatenate(
        [
            cell[:, None].astype(jnp.bfloat16),
            coords[1][:, None].astype(jnp.bfloat16),
            jnp.transpose(residuals[:, 0, 0, 0], (1, 0, 2)),
            weights[0, 0, 0][:, None],
            fraction[0, 0, 0][:, None],
        ],
        1,
    )
    incoming = lax.all_to_all(outgoing, "tf", 0, 0, tiled=True)
    idx = incoming[:, 0:2].astype(jnp.int32)
    values = incoming[:, 2:].astype(jnp.float32)
    weight_now = values[:, 3]
    share = values[:, 4]
    left_share = weight_now * (1.0 - share)
    right_share = weight_now * share
    dep = jnp.stack(
        [
            left_share,
            left_share * values[:, 0],
            left_share * values[:, 1],
            left_share * values[:, 2],
            right_share,
            right_share * values[:, 0],
            right_share * values[:, 1],
            right_share * values[:, 2],
        ],
        1,
    ).astype(jnp.bfloat16).astype(jnp.float32)
    raw = build_histogram(idx, dep, cell_rows)
    histogram = raw.reshape(cell_rows, 4, PAD_SLOT)[:cell_count, :, :PAD]
    histogram = histogram.reshape(drift_dev, row_dev, 4, PAD)
    means = histogram[:, :, 1:4] / (histogram[:, :, 0:1] + 1.0)
    means = jnp.transpose(means, (2, 0, 1, 3))
    field = smooth(means, kernel_reach)
    carried = exclusive_prefix(jnp.sum(field, axis=1))
    return carried[:, None] + jnp.cumsum(field, axis=1)


def solution(mesh):
    placed = (
        P(None, "tf", "gz", "sec", None, None),
        P("tf", "gz", "sec", None, None),
        P("tf", "gz", "sec", None, None),
        P(None, "tf", "gz", "sec", None, None),
        P("sec"),
    )
    return jax.shard_map(
        per_device,
        mesh=mesh,
        in_specs=placed,
        out_specs=P(None, ("tf", "gz"), "sec", None),
        check_vma=False,
    )
```

```python
import functools

import jax
import jax.numpy as jnp
from jax import lax
from jax.experimental import pallas as pl
from jax.experimental.pallas import tpu as pltpu
from jax.sharding import PartitionSpec as P

PAD = 180
DRIFT = 256
PAD_SLOT = 192
CHUNK = 4096


def with_halo(block, sides, width):
    for axis, dim in sides:
        count = lax.axis_size(axis)
        forward = [(i, i + 1) for i in range(count - 1)]
        backward = [(target, source) for source, target in forward]
        low = lax.ppermute(
            lax.slice_in_dim(block, block.shape[dim] - width, None, axis=dim), axis, forward
        )
        high = lax.ppermute(lax.slice_in_dim(block, 0, width, axis=dim), axis, backward)
        block = jnp.concatenate([low, block, high], axis=dim)
    return block


def row_kernels(kernel_reach):
    spread = kernel_reach.astype(jnp.float32)[:, None, None]
    places = lax.broadcasted_iota(jnp.int32, (PAD, PAD), 0)
    others = lax.broadcasted_iota(jnp.int32, (PAD, PAD), 1)
    distance = jnp.abs(places - others).astype(jnp.float32)[None]
    return jnp.maximum(spread + 1.0 - distance, 0.0) / ((spread + 1.0) * (spread + 1.0))


def hist_kernel(cell_rows, idx_ref, dep_ref, out_ref):
    source = pl.program_id(0)

    @pl.when(source == 0)
    def _():
        out_ref[...] = jnp.zeros_like(out_ref)

    length = idx_ref.shape[2]
    zero = jnp.zeros((), jnp.bfloat16)
    one = jnp.ones((), jnp.bfloat16)

    def body(step, carry):
        off = pl.multiple_of(step * CHUNK, CHUNK)
        cell = idx_ref[0, 0:1, pl.ds(off, CHUNK)].astype(jnp.bfloat16)
        pad = idx_ref[0, 1:2, pl.ds(off, CHUNK)].astype(jnp.bfloat16)
        dep = dep_ref[0, :, pl.ds(off, CHUNK)].astype(jnp.bfloat16)
        c_iota = lax.broadcasted_iota(jnp.int32, (cell_rows, CHUNK), 0).astype(jnp.bfloat16)
        onehot = jnp.where(c_iota == cell, one, zero)
        p_iota = lax.broadcasted_iota(jnp.int32, (PAD_SLOT, CHUNK), 0).astype(jnp.bfloat16)
        at_left = p_iota == pad
        at_right = p_iota == pad + one
        parts = []
        for k in range(4):
            parts.append(
                jnp.where(at_left, dep[k : k + 1], jnp.where(at_right, dep[4 + k : 5 + k], zero))
            )
        spread = jnp.concatenate(parts, 0)
        out_ref[...] += lax.dot_general(
            spread, onehot, (((1,), (1,)), ((), ())), preferred_element_type=jnp.float32
        )
        return carry

    lax.fori_loop(0, length // CHUNK, body, 0)


def build_histogram(idx, dep, cell_rows):
    sources, _, length = idx.shape
    flops = 2 * cell_rows * 4 * PAD_SLOT * sources * length
    return pl.pallas_call(
        functools.partial(hist_kernel, cell_rows),
        out_shape=jax.ShapeDtypeStruct((4 * PAD_SLOT, cell_rows), jnp.float32),
        grid=(sources,),
        in_specs=[
            pl.BlockSpec((1, 2, length), lambda s: (s, 0, 0)),
            pl.BlockSpec((1, 8, length), lambda s: (s, 0, 0)),
        ],
        out_specs=pl.BlockSpec((4 * PAD_SLOT, cell_rows), lambda s: (0, 0)),
        compiler_params=pltpu.CompilerParams(dimension_semantics=("arbitrary",)),
        cost_estimate=pl.CostEstimate(
            flops=flops,
            transcendentals=0,
            bytes_accessed=sources * length * 40 + cell_rows * 4 * PAD_SLOT * 4,
        ),
    )(idx, dep)


def exclusive_prefix(totals):
    gz_count = lax.axis_size("gz")
    tf_count = lax.axis_size("tf")
    g = lax.axis_index("gz")
    before = jnp.zeros_like(totals)
    row_sum = totals
    for shift in range(1, gz_count):
        pairs = [(i, (i + shift) % gz_count) for i in range(gz_count)]
        got = lax.ppermute(totals, "gz", pairs)
        row_sum = row_sum + got
        before = before + jnp.where(shift <= g, got, 0.0)
    for shift in range(1, tf_count):
        pairs = [(i, i + shift) for i in range(tf_count - shift)]
        before = before + lax.ppermute(row_sum, "tf", pairs)
    return before


def smooth(field, kernel_reach):
    across = jnp.einsum(
        "kzrq,rpq->kzrp", field, row_kernels(kernel_reach), precision=lax.Precision.HIGHEST
    )
    rimmed = with_halo(across, (("sec", 2),), 2)
    row_total = across.shape[2]
    return (
        rimmed[:, :, 0:row_total]
        + 2.0 * rimmed[:, :, 1 : row_total + 1]
        + 3.0 * rimmed[:, :, 2 : row_total + 2]
        + 2.0 * rimmed[:, :, 3 : row_total + 3]
        + rimmed[:, :, 4 : row_total + 4]
    ) / 9.0


def per_device(residuals, weights, fraction, voxels, kernel_reach):
    gz_count = lax.axis_size("gz")
    drift_dev = DRIFT // (lax.axis_size("tf") * gz_count)
    row_dev = kernel_reach.shape[0]
    cell_count = drift_dev * row_dev
    cell_rows = -(-cell_count // 16) * 16
    coords = voxels[:, 0, 0, 0]
    target = lax.broadcasted_iota(jnp.int32, coords.shape[1:], 0)
    local_row = coords[0] - lax.axis_index("sec") * row_dev
    local_drift = coords[2] - (target * gz_count + lax.axis_index("gz")) * drift_dev
    cell = local_drift * row_dev + local_row
    outgoing = jnp.concatenate(
        [
            cell[:, None].astype(jnp.bfloat16),
            coords[1][:, None].astype(jnp.bfloat16),
            jnp.transpose(residuals[:, 0, 0, 0], (1, 0, 2)),
            weights[0, 0, 0][:, None],
            fraction[0, 0, 0][:, None],
        ],
        1,
    )
    incoming = lax.all_to_all(outgoing, "tf", 0, 0, tiled=True)
    idx = incoming[:, 0:2].astype(jnp.int32)
    values = incoming[:, 2:].astype(jnp.float32)
    weight_now = values[:, 3]
    share = values[:, 4]
    left_share = weight_now * (1.0 - share)
    right_share = weight_now * share
    dep = jnp.stack(
        [
            left_share,
            left_share * values[:, 0],
            left_share * values[:, 1],
            left_share * values[:, 2],
            right_share,
            right_share * values[:, 0],
            right_share * values[:, 1],
            right_share * values[:, 2],
        ],
        1,
    ).astype(jnp.bfloat16).astype(jnp.float32)
    raw = build_histogram(idx, dep, cell_rows)
    histogram = raw.T.reshape(cell_rows, 4, PAD_SLOT)[:cell_count, :, :PAD]
    histogram = histogram.reshape(drift_dev, row_dev, 4, PAD)
    means = histogram[:, :, 1:4] / (histogram[:, :, 0:1] + 1.0)
    means = jnp.transpose(means, (2, 0, 1, 3))
    field = smooth(means, kernel_reach)
    carried = exclusive_prefix(jnp.sum(field, axis=1))
    return carried[:, None] + jnp.cumsum(field, axis=1)


def solution(mesh):
    placed = (
        P(None, "tf", "gz", "sec", None, None),
        P("tf", "gz", "sec", None, None),
        P("tf", "gz", "sec", None, None),
        P(None, "tf", "gz", "sec", None, None),
        P("sec"),
    )
    return jax.shard_map(
        per_device,
        mesh=mesh,
        in_specs=placed,
        out_specs=P(None, ("tf", "gz"), "sec", None),
        check_vma=False,
    )
```

```python
import functools

import jax
import jax.numpy as jnp
from jax import lax
from jax.experimental import pallas as pl
from jax.experimental.pallas import tpu as pltpu
from jax.sharding import PartitionSpec as P

PAD = 180
DRIFT = 256
PAD_SLOT = 192
CHUNK = 4096


def with_halo(block, sides, width):
    for axis, dim in sides:
        count = lax.axis_size(axis)
        forward = [(i, i + 1) for i in range(count - 1)]
        backward = [(target, source) for source, target in forward]
        low = lax.ppermute(
            lax.slice_in_dim(block, block.shape[dim] - width, None, axis=dim), axis, forward
        )
        high = lax.ppermute(lax.slice_in_dim(block, 0, width, axis=dim), axis, backward)
        block = jnp.concatenate([low, block, high], axis=dim)
    return block


def row_kernels(kernel_reach):
    spread = kernel_reach.astype(jnp.float32)[:, None, None]
    places = lax.broadcasted_iota(jnp.int32, (PAD, PAD), 0)
    others = lax.broadcasted_iota(jnp.int32, (PAD, PAD), 1)
    distance = jnp.abs(places - others).astype(jnp.float32)[None]
    return jnp.maximum(spread + 1.0 - distance, 0.0) / ((spread + 1.0) * (spread + 1.0))


def hist_kernel(cell_rows, first, order_ref, rows_ref, *rest):
    out_ref = rest[-1]

    @pl.when(pl.program_id(0) == 0)
    def _():
        if first:
            out_ref[...] = jnp.zeros_like(out_ref)
        else:
            out_ref[...] = rest[0][...]

    length = rows_ref.shape[2]
    zero = jnp.zeros((), jnp.bfloat16)
    one = jnp.ones((), jnp.bfloat16)

    def body(step, carry):
        off = pl.multiple_of(step * CHUNK, CHUNK)
        rows = rows_ref[0, :, pl.ds(off, CHUNK)].astype(jnp.float32)
        cell = rows[0:1].astype(jnp.bfloat16)
        pad = rows[1:2].astype(jnp.bfloat16)
        weight_now = rows[5:6]
        share = rows[6:7]
        left_share = weight_now * (1.0 - share)
        right_share = weight_now * share
        c_iota = lax.broadcasted_iota(jnp.int32, (cell_rows, CHUNK), 0).astype(jnp.bfloat16)
        onehot = jnp.where(c_iota == cell, one, zero)
        p_iota = lax.broadcasted_iota(jnp.int32, (PAD_SLOT, CHUNK), 0).astype(jnp.bfloat16)
        at_left = p_iota == pad
        at_right = p_iota == pad + one
        parts = []
        for k in range(4):
            if k == 0:
                left, right = left_share, right_share
            else:
                left, right = left_share * rows[k + 1 : k + 2], right_share * rows[k + 1 : k + 2]
            left = left.astype(jnp.bfloat16)
            right = right.astype(jnp.bfloat16)
            parts.append(jnp.where(at_left, left, jnp.where(at_right, right, zero)))
        spread = jnp.concatenate(parts, 0)
        out_ref[...] += lax.dot_general(
            spread, onehot, (((1,), (1,)), ((), ())), preferred_element_type=jnp.float32
        )
        return carry

    lax.fori_loop(0, length // CHUNK, body, 0)


def build_histogram(order, rows, steps, cell_rows, partial=None):
    sources, features, length = rows.shape
    first = partial is None
    flops = 2 * cell_rows * 4 * PAD_SLOT * steps * length
    in_specs = [pl.BlockSpec((1, features, length), lambda s, o: (o[s], 0, 0))]
    operands = [order, rows]
    aliases = {}
    if not first:
        in_specs.append(pl.BlockSpec((4 * PAD_SLOT, cell_rows), lambda s, o: (0, 0)))
        operands.append(partial)
        aliases = {2: 0}
    return pl.pallas_call(
        functools.partial(hist_kernel, cell_rows, first),
        out_shape=jax.ShapeDtypeStruct((4 * PAD_SLOT, cell_rows), jnp.float32),
        grid_spec=pltpu.PrefetchScalarGridSpec(
            num_scalar_prefetch=1,
            grid=(steps,),
            in_specs=in_specs,
            out_specs=pl.BlockSpec((4 * PAD_SLOT, cell_rows), lambda s, o: (0, 0)),
        ),
        input_output_aliases=aliases,
        compiler_params=pltpu.CompilerParams(dimension_semantics=("arbitrary",)),
        cost_estimate=pl.CostEstimate(
            flops=flops,
            transcendentals=0,
            bytes_accessed=steps * length * features * 2 + cell_rows * 4 * PAD_SLOT * 8,
        ),
    )(*operands)


def exclusive_prefix(totals):
    gz_count = lax.axis_size("gz")
    tf_count = lax.axis_size("tf")
    g = lax.axis_index("gz")
    before = jnp.zeros_like(totals)
    row_sum = totals
    for shift in range(1, gz_count):
        pairs = [(i, (i + shift) % gz_count) for i in range(gz_count)]
        got = lax.ppermute(totals, "gz", pairs)
        row_sum = row_sum + got
        before = before + jnp.where(shift <= g, got, 0.0)
    for shift in range(1, tf_count):
        pairs = [(i, i + shift) for i in range(tf_count - shift)]
        before = before + lax.ppermute(row_sum, "tf", pairs)
    return before


def smooth(field, kernel_reach):
    across = jnp.einsum(
        "kzrq,rpq->kzrp", field, row_kernels(kernel_reach), precision=lax.Precision.HIGHEST
    )
    rimmed = with_halo(across, (("sec", 2),), 2)
    row_total = across.shape[2]
    return (
        rimmed[:, :, 0:row_total]
        + 2.0 * rimmed[:, :, 1 : row_total + 1]
        + 3.0 * rimmed[:, :, 2 : row_total + 2]
        + 2.0 * rimmed[:, :, 3 : row_total + 3]
        + rimmed[:, :, 4 : row_total + 4]
    ) / 9.0


def per_device(residuals, weights, fraction, voxels, kernel_reach):
    gz_count = lax.axis_size("gz")
    drift_dev = DRIFT // (lax.axis_size("tf") * gz_count)
    row_dev = kernel_reach.shape[0]
    cell_count = drift_dev * row_dev
    cell_rows = -(-cell_count // 16) * 16
    coords = voxels[:, 0, 0, 0]
    target = lax.broadcasted_iota(jnp.int32, coords.shape[1:], 0)
    local_row = coords[0] - lax.axis_index("sec") * row_dev
    local_drift = coords[2] - (target * gz_count + lax.axis_index("gz")) * drift_dev
    cell = local_drift * row_dev + local_row
    outgoing = jnp.concatenate(
        [
            cell[:, None].astype(jnp.bfloat16),
            coords[1][:, None].astype(jnp.bfloat16),
            jnp.transpose(residuals[:, 0, 0, 0], (1, 0, 2)),
            weights[0, 0, 0][:, None],
            fraction[0, 0, 0][:, None],
        ],
        1,
    )
    incoming = lax.all_to_all(outgoing, "tf", 0, 0, tiled=True)
    tf_count = lax.axis_size("tf")
    here = lax.axis_index("tf")
    local = build_histogram(here[None], outgoing, 1, cell_rows)
    others = (here + lax.broadcasted_iota(jnp.int32, (tf_count - 1,), 0) + 1) % tf_count
    raw = build_histogram(others, incoming, tf_count - 1, cell_rows, local)
    histogram = raw.T.reshape(cell_rows, 4, PAD_SLOT)[:cell_count, :, :PAD]
    histogram = histogram.reshape(drift_dev, row_dev, 4, PAD)
    means = histogram[:, :, 1:4] / (histogram[:, :, 0:1] + 1.0)
    means = jnp.transpose(means, (2, 0, 1, 3))
    field = smooth(means, kernel_reach)
    carried = exclusive_prefix(jnp.sum(field, axis=1))
    return carried[:, None] + jnp.cumsum(field, axis=1)


def solution(mesh):
    placed = (
        P(None, "tf", "gz", "sec", None, None),
        P("tf", "gz", "sec", None, None),
        P("tf", "gz", "sec", None, None),
        P(None, "tf", "gz", "sec", None, None),
        P("sec"),
    )
    return jax.shard_map(
        per_device,
        mesh=mesh,
        in_specs=placed,
        out_specs=P(None, ("tf", "gz"), "sec", None),
        check_vma=False,
    )
```

```python
import functools

import jax
import jax.numpy as jnp
from jax import lax
from jax.experimental import pallas as pl
from jax.experimental.pallas import tpu as pltpu
from jax.sharding import PartitionSpec as P

PAD = 180
DRIFT = 256
PAD_SLOT = 192
CHUNK = 4096


def row_kernels(kernel_reach):
    spread = kernel_reach.astype(jnp.float32)[:, None, None]
    places = lax.broadcasted_iota(jnp.int32, (PAD, PAD), 0)
    others = lax.broadcasted_iota(jnp.int32, (PAD, PAD), 1)
    distance = jnp.abs(places - others).astype(jnp.float32)[None]
    return jnp.maximum(spread + 1.0 - distance, 0.0) / ((spread + 1.0) * (spread + 1.0))


def hist_kernel(cell_rows, first, order_ref, rows_ref, *rest):
    out_ref = rest[-1]

    @pl.when(pl.program_id(0) == 0)
    def _():
        if first:
            out_ref[...] = jnp.zeros_like(out_ref)
        else:
            out_ref[...] = rest[0][...]

    length = rows_ref.shape[2]
    zero = jnp.zeros((), jnp.bfloat16)
    one = jnp.ones((), jnp.bfloat16)

    def body(step, carry):
        off = pl.multiple_of(step * CHUNK, CHUNK)
        rows = rows_ref[0, :, pl.ds(off, CHUNK)].astype(jnp.float32)
        cell = rows[0:1].astype(jnp.bfloat16)
        pad = rows[1:2].astype(jnp.bfloat16)
        weight_now = rows[5:6]
        share = rows[6:7]
        left_share = weight_now * (1.0 - share)
        right_share = weight_now * share
        c_iota = lax.broadcasted_iota(jnp.int32, (cell_rows, CHUNK), 0).astype(jnp.bfloat16)
        onehot = jnp.where(c_iota == cell, one, zero)
        p_iota = lax.broadcasted_iota(jnp.int32, (PAD_SLOT, CHUNK), 0).astype(jnp.bfloat16)
        at_left = p_iota == pad
        at_right = p_iota == pad + one
        parts = []
        for k in range(4):
            if k == 0:
                left, right = left_share, right_share
            else:
                left, right = left_share * rows[k + 1 : k + 2], right_share * rows[k + 1 : k + 2]
            left = left.astype(jnp.bfloat16)
            right = right.astype(jnp.bfloat16)
            parts.append(jnp.where(at_left, left, jnp.where(at_right, right, zero)))
        spread = jnp.concatenate(parts, 0)
        out_ref[...] += lax.dot_general(
            spread, onehot, (((1,), (1,)), ((), ())), preferred_element_type=jnp.float32
        )
        return carry

    lax.fori_loop(0, length // CHUNK, body, 0)


def build_histogram(order, rows, steps, cell_rows, partial=None):
    sources, features, length = rows.shape
    first = partial is None
    flops = 2 * cell_rows * 4 * PAD_SLOT * steps * length
    in_specs = [pl.BlockSpec((1, features, length), lambda s, o: (o[s], 0, 0))]
    operands = [order, rows]
    aliases = {}
    if not first:
        in_specs.append(pl.BlockSpec((4 * PAD_SLOT, cell_rows), lambda s, o: (0, 0)))
        operands.append(partial)
        aliases = {2: 0}
    return pl.pallas_call(
        functools.partial(hist_kernel, cell_rows, first),
        out_shape=jax.ShapeDtypeStruct((4 * PAD_SLOT, cell_rows), jnp.float32),
        grid_spec=pltpu.PrefetchScalarGridSpec(
            num_scalar_prefetch=1,
            grid=(steps,),
            in_specs=in_specs,
            out_specs=pl.BlockSpec((4 * PAD_SLOT, cell_rows), lambda s, o: (0, 0)),
        ),
        input_output_aliases=aliases,
        compiler_params=pltpu.CompilerParams(dimension_semantics=("arbitrary",)),
        cost_estimate=pl.CostEstimate(
            flops=flops,
            transcendentals=0,
            bytes_accessed=steps * length * features * 2 + cell_rows * 4 * PAD_SLOT * 8,
        ),
    )(*operands)


def exclusive_prefix(totals):
    before = jnp.zeros_like(totals)
    group = totals
    for axis in ("gz", "tf"):
        count = lax.axis_size(axis)
        me = lax.axis_index(axis)
        mask = 1
        while mask < count:
            pairs = [(i, i ^ mask) for i in range(count)]
            got = lax.ppermute(group, axis, pairs)
            before = before + jnp.where((me & mask) != 0, got, 0.0)
            group = group + got
            mask *= 2
        if axis == "gz":
            before_row, before, group = before, jnp.zeros_like(totals), group
    return before_row + before


def per_device(residuals, weights, fraction, voxels, kernel_reach):
    gz_count = lax.axis_size("gz")
    drift_dev = DRIFT // (lax.axis_size("tf") * gz_count)
    row_dev = kernel_reach.shape[0]
    cell_count = drift_dev * row_dev
    cell_rows = -(-cell_count // 16) * 16
    coords = voxels[:, 0, 0, 0]
    target = lax.broadcasted_iota(jnp.int32, coords.shape[1:], 0)
    local_row = coords[0] - lax.axis_index("sec") * row_dev
    local_drift = coords[2] - (target * gz_count + lax.axis_index("gz")) * drift_dev
    cell = local_drift * row_dev + local_row
    outgoing = jnp.concatenate(
        [
            cell[:, None].astype(jnp.bfloat16),
            coords[1][:, None].astype(jnp.bfloat16),
            jnp.transpose(residuals[:, 0, 0, 0], (1, 0, 2)),
            weights[0, 0, 0][:, None],
            fraction[0, 0, 0][:, None],
        ],
        1,
    )
    incoming = lax.all_to_all(outgoing, "tf", 0, 0, tiled=True)
    tf_count = lax.axis_size("tf")
    here = lax.axis_index("tf")
    local = build_histogram(here[None], outgoing, 1, cell_rows)
    others = (here + lax.broadcasted_iota(jnp.int32, (tf_count - 1,), 0) + 1) % tf_count
    raw = build_histogram(others, incoming, tf_count - 1, cell_rows, local)
    histogram = raw.T.reshape(cell_rows, 4, PAD_SLOT)[:cell_count, :, :PAD]
    histogram = histogram.reshape(drift_dev, row_dev, 4, PAD)
    means = histogram[:, :, 1:4] / (histogram[:, :, 0:1] + 1.0)
    means = jnp.transpose(means, (2, 0, 1, 3))
    return finish(means, kernel_reach)


def pad_smooth(field, kernels):
    return jnp.einsum("...rq,rpq->...rp", field, kernels, precision=lax.Precision.HIGHEST)


def row_smooth(rimmed, row_total, axis):
    part = lambda start: lax.slice_in_dim(rimmed, start, start + row_total, axis=axis)
    return (part(0) + 2.0 * part(1) + 3.0 * part(2) + 2.0 * part(3) + part(4)) / 9.0


def finish(means, kernel_reach):
    count = lax.axis_size("sec")
    forward = [(i, i + 1) for i in range(count - 1)]
    backward = [(target, source) for source, target in forward]
    kernels = row_kernels(kernel_reach)
    row_total = kernels.shape[0]
    top = pad_smooth(means[:, :, row_total - 2 :], kernels[row_total - 2 :])
    bottom = pad_smooth(means[:, :, :2], kernels[:2])
    low = lax.ppermute(top, "sec", forward)
    high = lax.ppermute(bottom, "sec", backward)
    summed = pad_smooth(jnp.sum(means, axis=1), kernels)
    rim_sum = jnp.concatenate([jnp.sum(low, axis=1), summed, jnp.sum(high, axis=1)], axis=1)
    carried = exclusive_prefix(row_smooth(rim_sum, row_total, 1))
    across = pad_smooth(means, kernels)
    field = row_smooth(jnp.concatenate([low, across, high], axis=2), row_total, 2)
    return carried[:, None] + jnp.cumsum(field, axis=1)


def solution(mesh):
    placed = (
        P(None, "tf", "gz", "sec", None, None),
        P("tf", "gz", "sec", None, None),
        P("tf", "gz", "sec", None, None),
        P(None, "tf", "gz", "sec", None, None),
        P("sec"),
    )
    return jax.shard_map(
        per_device,
        mesh=mesh,
        in_specs=placed,
        out_specs=P(None, ("tf", "gz"), "sec", None),
        check_vma=False,
    )
```

```python
import functools

import jax
import jax.numpy as jnp
from jax import lax
from jax.experimental import pallas as pl
from jax.experimental.pallas import tpu as pltpu
from jax.sharding import PartitionSpec as P

PAD = 180
DRIFT = 256
PAD_SLOT = 192
CHUNK = 4096


def row_kernels(kernel_reach):
    spread = kernel_reach.astype(jnp.float32)[:, None, None]
    places = lax.broadcasted_iota(jnp.int32, (PAD, PAD), 0)
    others = lax.broadcasted_iota(jnp.int32, (PAD, PAD), 1)
    distance = jnp.abs(places - others).astype(jnp.float32)[None]
    return jnp.maximum(spread + 1.0 - distance, 0.0) / ((spread + 1.0) * (spread + 1.0))


def hist_kernel(cell_rows, first, order_ref, rows_ref, *rest):
    out_ref = rest[-1]

    @pl.when(pl.program_id(0) == 0)
    def _():
        if first:
            out_ref[...] = jnp.zeros_like(out_ref)
        else:
            out_ref[...] = rest[0][...]

    length = rows_ref.shape[2]
    zero = jnp.zeros((), jnp.bfloat16)
    one = jnp.ones((), jnp.bfloat16)

    def body(step, carry):
        off = pl.multiple_of(step * CHUNK, CHUNK)
        rows = rows_ref[0, :, pl.ds(off, CHUNK)].astype(jnp.float32)
        cell = rows[0:1].astype(jnp.bfloat16)
        pad = rows[1:2].astype(jnp.bfloat16)
        weight_now = rows[5:6]
        share = rows[6:7]
        left_share = weight_now * (1.0 - share)
        right_share = weight_now * share
        c_iota = lax.broadcasted_iota(jnp.int32, (cell_rows, CHUNK), 0).astype(jnp.bfloat16)
        onehot = jnp.where(c_iota == cell, one, zero)
        p_iota = lax.broadcasted_iota(jnp.int32, (PAD_SLOT, CHUNK), 0).astype(jnp.bfloat16)
        at_left = p_iota == pad
        at_right = p_iota == pad + one
        parts = []
        for k in range(4):
            if k == 0:
                left, right = left_share, right_share
            else:
                left, right = left_share * rows[k + 1 : k + 2], right_share * rows[k + 1 : k + 2]
            left = left.astype(jnp.bfloat16)
            right = right.astype(jnp.bfloat16)
            parts.append(jnp.where(at_left, left, jnp.where(at_right, right, zero)))
        spread = jnp.concatenate(parts, 0)
        out_ref[...] += lax.dot_general(
            spread, onehot, (((1,), (1,)), ((), ())), preferred_element_type=jnp.float32
        )
        return carry

    lax.fori_loop(0, length // CHUNK, body, 0)


def build_histogram(order, rows, steps, cell_rows, partial=None):
    sources, features, length = rows.shape
    first = partial is None
    flops = 2 * cell_rows * 4 * PAD_SLOT * steps * length
    in_specs = [pl.BlockSpec((1, features, length), lambda s, o: (o[s], 0, 0))]
    operands = [order, rows]
    aliases = {}
    if not first:
        in_specs.append(pl.BlockSpec((4 * PAD_SLOT, cell_rows), lambda s, o: (0, 0)))
        operands.append(partial)
        aliases = {2: 0}
    return pl.pallas_call(
        functools.partial(hist_kernel, cell_rows, first),
        out_shape=jax.ShapeDtypeStruct((4 * PAD_SLOT, cell_rows), jnp.float32),
        grid_spec=pltpu.PrefetchScalarGridSpec(
            num_scalar_prefetch=1,
            grid=(steps,),
            in_specs=in_specs,
            out_specs=pl.BlockSpec((4 * PAD_SLOT, cell_rows), lambda s, o: (0, 0)),
        ),
        input_output_aliases=aliases,
        compiler_params=pltpu.CompilerParams(dimension_semantics=("arbitrary",)),
        cost_estimate=pl.CostEstimate(
            flops=flops,
            transcendentals=0,
            bytes_accessed=steps * length * features * 2 + cell_rows * 4 * PAD_SLOT * 8,
        ),
    )(*operands)


SCAN_ROUNDS = {'gz': ((1,), (2, 4, 6)), 'tf': ((1, 2, 3),)}


def scan_axis(group, axis, rounds):
    me = lax.axis_index(axis)
    count = lax.axis_size(axis)
    before = jnp.zeros_like(group)
    for masks in rounds:
        bits = functools.reduce(lambda x, y: x | y, masks)
        got = [lax.ppermute(group, axis, [(i, i ^ m) for i in range(count)]) for m in masks]
        for m, part in zip(masks, got):
            lower = ((me ^ m) & bits) < (me & bits)
            before = before + jnp.where(lower, part, 0.0)
        group = group + functools.reduce(lambda x, y: x + y, got)
    return before, group


def exclusive_prefix(totals):
    before_row, row_sum = scan_axis(totals, "gz", SCAN_ROUNDS["gz"])
    before_col, _ = scan_axis(row_sum, "tf", SCAN_ROUNDS["tf"])
    return before_row + before_col


def per_device(residuals, weights, fraction, voxels, kernel_reach):
    gz_count = lax.axis_size("gz")
    drift_dev = DRIFT // (lax.axis_size("tf") * gz_count)
    row_dev = kernel_reach.shape[0]
    cell_count = drift_dev * row_dev
    cell_rows = -(-cell_count // 16) * 16
    coords = voxels[:, 0, 0, 0]
    target = lax.broadcasted_iota(jnp.int32, coords.shape[1:], 0)
    local_row = coords[0] - lax.axis_index("sec") * row_dev
    local_drift = coords[2] - (target * gz_count + lax.axis_index("gz")) * drift_dev
    cell = local_drift * row_dev + local_row
    outgoing = jnp.concatenate(
        [
            cell[:, None].astype(jnp.bfloat16),
            coords[1][:, None].astype(jnp.bfloat16),
            jnp.transpose(residuals[:, 0, 0, 0], (1, 0, 2)),
            weights[0, 0, 0][:, None],
            fraction[0, 0, 0][:, None],
        ],
        1,
    )
    incoming = lax.all_to_all(outgoing, "tf", 0, 0, tiled=True)
    tf_count = lax.axis_size("tf")
    here = lax.axis_index("tf")
    local = build_histogram(here[None], outgoing, 1, cell_rows)
    others = (here + lax.broadcasted_iota(jnp.int32, (tf_count - 1,), 0) + 1) % tf_count
    raw = build_histogram(others, incoming, tf_count - 1, cell_rows, local)
    histogram = raw.T.reshape(cell_rows, 4, PAD_SLOT)[:cell_count, :, :PAD]
    histogram = histogram.reshape(drift_dev, row_dev, 4, PAD)
    means = histogram[:, :, 1:4] / (histogram[:, :, 0:1] + 1.0)
    means = jnp.transpose(means, (2, 0, 1, 3))
    return finish(means, kernel_reach)


def pad_smooth(field, kernels):
    return jnp.einsum("...rq,rpq->...rp", field, kernels, precision=lax.Precision.HIGHEST)


def row_smooth(rimmed, row_total, axis):
    part = lambda start: lax.slice_in_dim(rimmed, start, start + row_total, axis=axis)
    return (part(0) + 2.0 * part(1) + 3.0 * part(2) + 2.0 * part(3) + part(4)) / 9.0


def finish(means, kernel_reach):
    count = lax.axis_size("sec")
    forward = [(i, i + 1) for i in range(count - 1)]
    backward = [(target, source) for source, target in forward]
    kernels = row_kernels(kernel_reach)
    row_total = kernels.shape[0]
    top = pad_smooth(means[:, :, row_total - 2 :], kernels[row_total - 2 :])
    bottom = pad_smooth(means[:, :, :2], kernels[:2])
    low = lax.ppermute(top, "sec", forward)
    high = lax.ppermute(bottom, "sec", backward)
    summed = pad_smooth(jnp.sum(means, axis=1), kernels)
    rim_sum = jnp.concatenate([jnp.sum(low, axis=1), summed, jnp.sum(high, axis=1)], axis=1)
    carried = exclusive_prefix(row_smooth(rim_sum, row_total, 1))
    across = pad_smooth(means, kernels)
    field = row_smooth(jnp.concatenate([low, across, high], axis=2), row_total, 2)
    return carried[:, None] + jnp.cumsum(field, axis=1)


def solution(mesh):
    placed = (
        P(None, "tf", "gz", "sec", None, None),
        P("tf", "gz", "sec", None, None),
        P("tf", "gz", "sec", None, None),
        P(None, "tf", "gz", "sec", None, None),
        P("sec"),
    )
    return jax.shard_map(
        per_device,
        mesh=mesh,
        in_specs=placed,
        out_specs=P(None, ("tf", "gz"), "sec", None),
        check_vma=False,
    )
```

```python
import functools

import jax
import jax.numpy as jnp
from jax import lax
from jax.experimental import pallas as pl
from jax.experimental.pallas import tpu as pltpu
from jax.sharding import PartitionSpec as P

PAD = 180
DRIFT = 256
PAD_SLOT = 192
CHUNK = 4096
MAX_REACH = 4


def row_taps(kernel_reach):
    spread = kernel_reach.astype(jnp.float32)[:, None]
    distance = jnp.abs(lax.broadcasted_iota(jnp.int32, (1, 2 * MAX_REACH + 1), 1) - MAX_REACH)
    return jnp.maximum(spread + 1.0 - distance.astype(jnp.float32), 0.0) / ((spread + 1.0) * (spread + 1.0))


def hist_kernel(cell_rows, first, order_ref, rows_ref, *rest):
    out_ref = rest[-1]

    @pl.when(pl.program_id(0) == 0)
    def _():
        if first:
            out_ref[...] = jnp.zeros_like(out_ref)
        else:
            out_ref[...] = rest[0][...]

    length = rows_ref.shape[2]
    zero = jnp.zeros((), jnp.bfloat16)
    one = jnp.ones((), jnp.bfloat16)

    def body(step, carry):
        off = pl.multiple_of(step * CHUNK, CHUNK)
        rows = rows_ref[0, :, pl.ds(off, CHUNK)].astype(jnp.float32)
        cell = rows[0:1].astype(jnp.bfloat16)
        pad = rows[1:2].astype(jnp.bfloat16)
        weight_now = rows[5:6]
        share = rows[6:7]
        left_share = weight_now * (1.0 - share)
        right_share = weight_now * share
        c_iota = lax.broadcasted_iota(jnp.int32, (cell_rows, CHUNK), 0).astype(jnp.bfloat16)
        onehot = jnp.where(c_iota == cell, one, zero)
        p_iota = lax.broadcasted_iota(jnp.int32, (PAD_SLOT, CHUNK), 0).astype(jnp.bfloat16)
        at_left = p_iota == pad
        at_right = p_iota == pad + one
        parts = []
        for k in range(4):
            if k == 0:
                left, right = left_share, right_share
            else:
                left, right = left_share * rows[k + 1 : k + 2], right_share * rows[k + 1 : k + 2]
            left = left.astype(jnp.bfloat16)
            right = right.astype(jnp.bfloat16)
            parts.append(jnp.where(at_left, left, jnp.where(at_right, right, zero)))
        spread = jnp.concatenate(parts, 0)
        out_ref[...] += lax.dot_general(
            spread, onehot, (((1,), (1,)), ((), ())), preferred_element_type=jnp.float32
        )
        return carry

    lax.fori_loop(0, length // CHUNK, body, 0)


def build_histogram(order, rows, steps, cell_rows, partial=None):
    sources, features, length = rows.shape
    first = partial is None
    flops = 2 * cell_rows * 4 * PAD_SLOT * steps * length
    in_specs = [pl.BlockSpec((1, features, length), lambda s, o: (o[s], 0, 0))]
    operands = [order, rows]
    aliases = {}
    if not first:
        in_specs.append(pl.BlockSpec((4 * PAD_SLOT, cell_rows), lambda s, o: (0, 0)))
        operands.append(partial)
        aliases = {2: 0}
    return pl.pallas_call(
        functools.partial(hist_kernel, cell_rows, first),
        out_shape=jax.ShapeDtypeStruct((4 * PAD_SLOT, cell_rows), jnp.float32),
        grid_spec=pltpu.PrefetchScalarGridSpec(
            num_scalar_prefetch=1,
            grid=(steps,),
            in_specs=in_specs,
            out_specs=pl.BlockSpec((4 * PAD_SLOT, cell_rows), lambda s, o: (0, 0)),
        ),
        input_output_aliases=aliases,
        compiler_params=pltpu.CompilerParams(dimension_semantics=("arbitrary",)),
        cost_estimate=pl.CostEstimate(
            flops=flops,
            transcendentals=0,
            bytes_accessed=steps * length * features * 2 + cell_rows * 4 * PAD_SLOT * 8,
        ),
    )(*operands)


SCAN_ROUNDS = {'gz': ((1,), (2, 4, 6)), 'tf': ((1, 2, 3),)}


def scan_axis(group, axis, rounds):
    me = lax.axis_index(axis)
    count = lax.axis_size(axis)
    before = jnp.zeros_like(group)
    for masks in rounds:
        bits = functools.reduce(lambda x, y: x | y, masks)
        got = [lax.ppermute(group, axis, [(i, i ^ m) for i in range(count)]) for m in masks]
        for m, part in zip(masks, got):
            lower = ((me ^ m) & bits) < (me & bits)
            before = before + jnp.where(lower, part, 0.0)
        group = group + functools.reduce(lambda x, y: x + y, got)
    return before, group


def exclusive_prefix(totals):
    before_row, row_sum = scan_axis(totals, "gz", SCAN_ROUNDS["gz"])
    before_col, _ = scan_axis(row_sum, "tf", SCAN_ROUNDS["tf"])
    return before_row + before_col


def per_device(residuals, weights, fraction, voxels, kernel_reach):
    gz_count = lax.axis_size("gz")
    drift_dev = DRIFT // (lax.axis_size("tf") * gz_count)
    row_dev = kernel_reach.shape[0]
    cell_count = drift_dev * row_dev
    cell_rows = -(-cell_count // 16) * 16
    coords = voxels[:, 0, 0, 0]
    target = lax.broadcasted_iota(jnp.int32, coords.shape[1:], 0)
    local_row = coords[0] - lax.axis_index("sec") * row_dev
    local_drift = coords[2] - (target * gz_count + lax.axis_index("gz")) * drift_dev
    cell = local_drift * row_dev + local_row
    outgoing = jnp.concatenate(
        [
            cell[:, None].astype(jnp.bfloat16),
            coords[1][:, None].astype(jnp.bfloat16),
            jnp.transpose(residuals[:, 0, 0, 0], (1, 0, 2)),
            weights[0, 0, 0][:, None],
            fraction[0, 0, 0][:, None],
        ],
        1,
    )
    incoming = lax.all_to_all(outgoing, "tf", 0, 0, tiled=True)
    tf_count = lax.axis_size("tf")
    here = lax.axis_index("tf")
    local = build_histogram(here[None], outgoing, 1, cell_rows)
    others = (here + lax.broadcasted_iota(jnp.int32, (tf_count - 1,), 0) + 1) % tf_count
    raw = build_histogram(others, incoming, tf_count - 1, cell_rows, local)
    histogram = raw.T.reshape(cell_rows, 4, PAD_SLOT)[:cell_count, :, :PAD]
    histogram = histogram.reshape(drift_dev, row_dev, 4, PAD)
    means = histogram[:, :, 1:4] / (histogram[:, :, 0:1] + 1.0)
    means = jnp.transpose(means, (2, 0, 1, 3))
    return finish(means, kernel_reach)


def pad_smooth(field, taps):
    reach = taps.shape[-1] // 2
    widths = [(0, 0)] * (field.ndim - 1) + [(reach, reach)]
    padded = jnp.pad(field, widths)
    total = field.shape[-1]
    out = taps[:, reach : reach + 1] * field
    for shift in range(-reach, reach + 1):
        if shift != 0:
            part = lax.slice_in_dim(padded, reach + shift, reach + shift + total, axis=field.ndim - 1)
            out = out + taps[:, reach + shift : reach + shift + 1] * part
    return out


def row_smooth(rimmed, row_total, axis):
    part = lambda start: lax.slice_in_dim(rimmed, start, start + row_total, axis=axis)
    return (part(0) + 2.0 * part(1) + 3.0 * part(2) + 2.0 * part(3) + part(4)) / 9.0


def finish(means, kernel_reach):
    count = lax.axis_size("sec")
    forward = [(i, i + 1) for i in range(count - 1)]
    backward = [(target, source) for source, target in forward]
    kernels = row_taps(kernel_reach)
    row_total = kernels.shape[0]
    top = pad_smooth(means[:, :, row_total - 2 :], kernels[row_total - 2 :])
    bottom = pad_smooth(means[:, :, :2], kernels[:2])
    low = lax.ppermute(top, "sec", forward)
    high = lax.ppermute(bottom, "sec", backward)
    summed = pad_smooth(jnp.sum(means, axis=1), kernels)
    rim_sum = jnp.concatenate([jnp.sum(low, axis=1), summed, jnp.sum(high, axis=1)], axis=1)
    carried = exclusive_prefix(row_smooth(rim_sum, row_total, 1))
    across = pad_smooth(means, kernels)
    field = row_smooth(jnp.concatenate([low, across, high], axis=2), row_total, 2)
    return carried[:, None] + jnp.cumsum(field, axis=1)


def solution(mesh):
    placed = (
        P(None, "tf", "gz", "sec", None, None),
        P("tf", "gz", "sec", None, None),
        P("tf", "gz", "sec", None, None),
        P(None, "tf", "gz", "sec", None, None),
        P("sec"),
    )
    return jax.shard_map(
        per_device,
        mesh=mesh,
        in_specs=placed,
        out_specs=P(None, ("tf", "gz"), "sec", None),
        check_vma=False,
    )
```
